256 devices in a mesh: rows: 16 (over x, y), sub: 16 (over z, core).
Axes of the slice: x: 4, y: 4, z: 8, core: 2. Of those that a mesh axis runs over, the one named last changes fastest.
Arguments:
- embeddings: bfloat16 [65536, 1024], P(('rows', 'sub'))
- codes: int32 [64, 65536], P(None, ('rows', 'sub')), may hold values from 0 to 255
- codebook: bfloat16 [256, 1024], P(None, 'sub'), may hold values from -6 to 6
Outputs:
- rotation: float32 [1024, 1024], P('sub')
- rotated: bfloat16 [65536, 1024], P(('rows', 'sub'))
- new_codebook: float32 [256, 1024], P(None, 'sub')
The draws below stay inside these ranges and needn't reach their ends.
All inputs are finite; a program needn't handle non-finite values.
Results may differ from the reference program's by a relative error of at most 0.0095.
Values may be sent and summed in bfloat16 or wider, within the bound.
No kernel may reach another device: no remote copies, remote signals or barrier semaphores. Data moves between devices by JAX's collectives and lax.ppermute only.
A program may use at most 64 MiB of HBM per device.

```python
import math
import jax
import jax.numpy as jnp
import numpy as np
from jax import lax

D = 1024
SUBSPACES = 64
K = 256
SUBDIM = 16
NS_STEPS = 3
ROW_DEV = 256
ROWS = 65536


def draw_embeddings(key, part):
    key_rows, key_cols, key_base = jax.random.split(key, 3)
    row_scale = jnp.exp(jax.random.uniform(key_rows, (ROWS, 1), jnp.float32) * math.log(10.0))
    col_scale = jnp.exp(jax.random.uniform(key_cols, (1, D), jnp.float32) * math.log(10.0))
    base = jax.random.normal(key_base, (ROWS, D), jnp.float32)
    return (0.2 * row_scale * col_scale * base).astype(jnp.bfloat16)


def set_ends(array, key, low, top_value):
    shape = array.shape
    place = [jax.random.randint(jax.random.fold_in(key, axis), (), 0, shape[axis]) for axis in range(len(shape))]
    array = array.at[tuple(place)].set(low)
    longest = shape.index(max(shape))
    place[longest] = (place[longest] + 1) % shape[longest]
    return array.at[tuple(place)].set(top_value)


def block_levels(stream_key, dims, cuts, smallest, largest):
    factor_of, own = 1.0, jax.random.fold_in(stream_key, 6)
    for axis_at, blocks in cuts:
        heights = jnp.exp(jax.random.uniform(jax.random.fold_in(own, axis_at), (blocks,), jnp.float32, smallest / len(cuts), largest / len(cuts)))
        factor_of = factor_of * jnp.repeat(heights, dims[axis_at] // blocks).reshape([-1 if axis == axis_at else 1 for axis in range(len(dims))])
    return factor_of


def rank_table(count, slope):
    portions = [(1 << 20) // math.isqrt(rank ** slope) + 1 for rank in range(1, count + 1)]
    scale = 1 + sum(portions) // (1 << 30)
    return np.cumsum(np.array([max(1, weight // scale) for weight in portions]))


def ranked_ids(stream_key, dims, amount, slope):
    table = rank_table(amount, slope)
    pick = jax.random.randint(jax.random.fold_in(stream_key, 1), dims, 0, int(table[amount - 1]))
    grade = jnp.searchsorted(jnp.asarray(table, jnp.int32), pick, side="right")
    return jax.random.permutation(jax.random.fold_in(stream_key, 2), amount)[grade].astype(jnp.int32)


def noise(key, extent, scale, most, cuts=(), held_as=jnp.bfloat16):
    result = jax.random.normal(key, extent, jnp.float32) * scale
    if len(cuts) > 0:
        result = block_levels(key, extent, cuts, -0.22, 0.18) * result
    return jnp.clip(result, min=-most, max=most).astype(held_as)


def setup_inputs(seed: int = 0) -> dict:
    splits = jax.random.split(jax.random.key(seed), 4)
    embeddings = draw_embeddings(jax.random.fold_in(splits[3], 71), 0)
    codes = set_ends(ranked_ids(splits[1], (SUBSPACES, ROWS), K, 3), jax.random.fold_in(splits[1], 3), 0, K - 1).astype(jnp.int32)
    codebook = noise(splits[2], (K, D), 1.0, 6.0, ((1, 16),))
    return {"embeddings": embeddings, "codes": codes, "codebook": codebook}


coef_a = 3.4445
coef_b = -4.775
coef_c = 2.0315
frob_eps = 1e-07
highest = lax.Precision.HIGHEST

def rows_dot(left, right):
    return lax.dot_general(left, right, (((1,), (1,)), ((), ())), precision=highest, preferred_element_type=jnp.float32)

def reference(embeddings, codes, codebook):
    block_rows = ROW_DEV
    blocks = ROWS // block_rows
    codewords = codebook.astype(jnp.float32).reshape(K, SUBSPACES, SUBDIM)
    row_blocks = embeddings.reshape(blocks, block_rows, D)
    code_blocks = codes.reshape(SUBSPACES, blocks, block_rows).transpose(1, 0, 2)
    subspace_ids = lax.broadcasted_iota(jnp.int32, (SUBSPACES, block_rows), 0)

    def cross_block(running, pieces):
        picked = codewords[pieces[1], subspace_ids, :]
        decoded = picked.transpose(1, 0, 2).reshape(block_rows, D).astype(jnp.bfloat16)
        block_term = jnp.dot(pieces[0].T, decoded, preferred_element_type=jnp.float32)
        return (running + block_term, None)
    cross_cov, unused = lax.scan(cross_block, jnp.zeros((D, D), jnp.float32), (row_blocks, code_blocks))
    frob_scale = jnp.sqrt(jnp.sum(cross_cov * cross_cov)) + frob_eps
    ortho_iter = cross_cov / frob_scale
    for newton_step in range(NS_STEPS):
        gram_rows = rows_dot(ortho_iter, ortho_iter)
        quartic = rows_dot(jnp.dot(gram_rows, ortho_iter, precision=highest, preferred_element_type=jnp.float32), ortho_iter)
        mixer = coef_b * gram_rows + coef_c * quartic
        ortho_iter = coef_a * ortho_iter + jnp.dot(mixer, ortho_iter, precision=highest, preferred_element_type=jnp.float32)
    rotation = ortho_iter
    rotation_half = rotation.astype(jnp.bfloat16)

    def rotate_block(running, pieces):
        rotated_block = jnp.dot(pieces[0], rotation_half, preferred_element_type=jnp.float32).astype(jnp.bfloat16)
        segment_ids = (pieces[1] + subspace_ids * K).T.reshape(block_rows * SUBSPACES)
        values = rotated_block.astype(jnp.float32).reshape(block_rows * SUBSPACES, SUBDIM)
        block_sums = jax.ops.segment_sum(values, segment_ids, num_segments=SUBSPACES * K)
        block_counts = jax.ops.segment_sum(jnp.ones((block_rows * SUBSPACES,), jnp.float32), segment_ids, num_segments=SUBSPACES * K)
        return ((running[0] + block_sums, running[1] + block_counts), rotated_block)
    initial = (jnp.zeros((SUBSPACES * K, SUBDIM), jnp.float32), jnp.zeros((SUBSPACES * K,), jnp.float32))
    (code_sums, counts), rotated = lax.scan(rotate_block, initial, (row_blocks, code_blocks))
    rotated = rotated.reshape(ROWS, D)
    code_sums = code_sums.reshape(SUBSPACES, K, SUBDIM).transpose(1, 0, 2).reshape(K, D)
    counts = counts.reshape(SUBSPACES, K).T
    spread = jnp.repeat(counts, SUBDIM, axis=1)
    new_codebook = (code_sums + codebook.astype(jnp.float32)) / (spread + 1.0)
    return (rotation, rotated, new_codebook)
```

```python
import math

import jax
import jax.numpy as jnp
from jax import lax
from jax.sharding import PartitionSpec as P

NS_STEPS = 3


coef_a = 3.4445
coef_b = -4.775
coef_c = 2.0315
frob_eps = 1e-07


def one_hot_codes(code_block, count_codes):
    levels = lax.broadcasted_iota(jnp.int32, code_block.shape + (count_codes,), 2)
    return (code_block[:, :, None] == levels).astype(jnp.bfloat16)


def decode_rows(codes, table):
    subspaces, local_rows = codes.shape
    count_codes, row_width = table.shape
    sub_width = row_width // subspaces
    codewords = table.reshape(count_codes, subspaces, sub_width)
    one_hot = one_hot_codes(codes, count_codes)
    picked = jnp.einsum("mnk,kmj->nmj", one_hot, codewords, preferred_element_type=jnp.float32)
    return picked.reshape(local_rows, row_width).astype(jnp.bfloat16)


def codeword_totals(codes, row_values, count_codes):
    subspaces, local_rows = codes.shape
    row_width = row_values.shape[1]
    sub_width = row_width // subspaces
    one_hot = one_hot_codes(codes, count_codes)
    pieces = row_values.reshape(local_rows, subspaces, sub_width)
    code_sums = jnp.einsum("mnk,nmj->kmj", one_hot, pieces, preferred_element_type=jnp.float32)
    counts = jnp.sum(one_hot, axis=1, dtype=jnp.float32).T
    return code_sums.reshape(count_codes, row_width), counts


def bdot(left, right, dims):
    return lax.dot_general(
        left.astype(jnp.bfloat16), right.astype(jnp.bfloat16), (dims, ((), ())),
        preferred_element_type=jnp.float32,
    )


def newton_step(z):
    z_half = z.astype(jnp.bfloat16)
    gram = bdot(z_half, z_half, ((1,), (1,)))
    quartic = bdot(gram, gram, ((1,), (0,)))
    mixer = coef_b * gram + coef_c * quartic
    return coef_a * z + bdot(mixer, z_half, ((1,), (0,)))


def body(embeddings, codes, codebook):
    table = lax.all_gather(codebook, "sub", axis=1, tiled=True)
    decoded = decode_rows(codes, table)
    partial = lax.dot_general(
        embeddings, decoded, (((0,), (0,)), ((), ())), preferred_element_type=jnp.float32
    )
    cross = lax.psum(partial, ("rows", "sub"))
    frob_scale = jnp.sqrt(jnp.sum(cross * cross)) + frob_eps
    z = cross / frob_scale
    for newton_step_index in range(NS_STEPS):
        z = newton_step(z)
    rotation_half = z.astype(jnp.bfloat16)
    rotated = jnp.dot(embeddings, rotation_half, preferred_element_type=jnp.float32).astype(
        jnp.bfloat16
    )
    code_sums, counts = codeword_totals(codes, rotated, table.shape[0])
    code_sums = lax.psum(code_sums, ("rows", "sub"))
    counts = lax.psum(counts, ("rows", "sub"))
    me = lax.axis_index("sub")
    cols = codebook.shape[1]
    own_subspaces = counts.shape[1] * cols // code_sums.shape[1]
    own_sums = lax.dynamic_slice_in_dim(code_sums, me * cols, cols, axis=1)
    own_counts = lax.dynamic_slice_in_dim(counts, me * own_subspaces, own_subspaces, axis=1)
    own_codebook = codebook.astype(jnp.float32)
    spread = jnp.repeat(own_counts, cols // own_subspaces, axis=1)
    new_codebook = (own_sums + own_codebook) / (spread + 1.0)
    panel_rows = z.shape[0] // lax.axis_size("sub")
    panel = lax.dynamic_slice_in_dim(z, me * panel_rows, panel_rows, axis=0)
    return (panel, rotated, new_codebook)


def solution(mesh):
    in_specs = (P(("rows", "sub"), None), P(None, ("rows", "sub")), P(None, "sub"))
    out_specs = (P("sub", None), P(("rows", "sub"), None), P(None, "sub"))
    return jax.shard_map(body, mesh=mesh, in_specs=in_specs, out_specs=out_specs, check_vma=False)
```

```python
import jax
import jax.numpy as jnp
from jax import lax
from jax.sharding import PartitionSpec as P

NS_STEPS = 3


coef_a = 3.4445
coef_b = -4.775
coef_c = 2.0315
frob_eps = 1e-07


def one_hot_codes(code_block, count_codes):
    levels = lax.broadcasted_iota(jnp.int32, code_block.shape + (count_codes,), 2)
    return (code_block[:, :, None] == levels).astype(jnp.bfloat16)


def decode_rows(codes, table):
    subspaces, local_rows = codes.shape
    count_codes, row_width = table.shape
    sub_width = row_width // subspaces
    codewords = table.reshape(count_codes, subspaces, sub_width)
    one_hot = one_hot_codes(codes, count_codes)
    picked = jnp.einsum("mnk,kmj->nmj", one_hot, codewords, preferred_element_type=jnp.float32)
    return picked.reshape(local_rows, row_width).astype(jnp.bfloat16)


def codeword_totals(codes, row_values, count_codes):
    subspaces, local_rows = codes.shape
    row_width = row_values.shape[1]
    sub_width = row_width // subspaces
    one_hot = one_hot_codes(codes, count_codes)
    pieces = row_values.reshape(local_rows, subspaces, sub_width)
    code_sums = jnp.einsum("mnk,nmj->kmj", one_hot, pieces, preferred_element_type=jnp.float32)
    counts = jnp.sum(one_hot, axis=1, dtype=jnp.float32).T
    return code_sums.reshape(count_codes, row_width), counts


def rows_sum(x):
    groups = lax.axis_size("rows")
    chunk = x.shape[0] // groups
    scattered = lax.all_to_all(x, "rows", split_axis=0, concat_axis=0, tiled=True)
    own = jnp.sum(scattered.reshape((groups, chunk) + x.shape[1:]), axis=0)
    spread = jnp.broadcast_to(own[None], (groups,) + own.shape).reshape(x.shape)
    return lax.all_to_all(spread, "rows", split_axis=0, concat_axis=0, tiled=True)


def bdot(left, right, dims):
    return lax.dot_general(
        left.astype(jnp.bfloat16), right.astype(jnp.bfloat16), (dims, ((), ())),
        preferred_element_type=jnp.float32,
    )


def newton_step(z):
    z_half = z.astype(jnp.bfloat16)
    gram = bdot(z_half, z_half, ((1,), (1,)))
    quartic = bdot(gram, gram, ((1,), (0,)))
    mixer = coef_b * gram + coef_c * quartic
    return coef_a * z + bdot(mixer, z_half, ((1,), (0,)))


def body(embeddings, codes, codebook):
    moved_codes = lax.all_to_all(codes, "sub", split_axis=0, concat_axis=1, tiled=True)
    table = lax.all_gather(codebook, "sub", axis=1, tiled=True)
    decoded = decode_rows(codes, table)
    partial = lax.dot_general(
        embeddings, decoded, (((0,), (0,)), ((), ())), preferred_element_type=jnp.float32
    )
    partial_panel = lax.psum_scatter(partial, "sub", scatter_dimension=0, tiled=True)
    cross_panel = rows_sum(partial_panel)
    cross = lax.all_gather(cross_panel, "sub", axis=0, tiled=True)
    frob_scale = jnp.sqrt(jnp.sum(cross * cross)) + frob_eps
    z = cross / frob_scale
    for newton_step_index in range(NS_STEPS):
        z = newton_step(z)
    rotation_half = z.astype(jnp.bfloat16)
    rotated = jnp.dot(embeddings, rotation_half, preferred_element_type=jnp.float32).astype(
        jnp.bfloat16
    )
    moved_rows = lax.all_to_all(rotated, "sub", split_axis=1, concat_axis=0, tiled=True)
    code_sums, counts = codeword_totals(moved_codes, moved_rows, table.shape[0])
    sums_width = code_sums.shape[1]
    totals = rows_sum(jnp.concatenate([code_sums, counts], axis=1))
    code_sums, counts = totals[:, :sums_width], totals[:, sums_width:]
    own_codebook = codebook.astype(jnp.float32)
    spread = jnp.repeat(counts, own_codebook.shape[1] // counts.shape[1], axis=1)
    new_codebook = (code_sums + own_codebook) / (spread + 1.0)
    me = lax.axis_index("sub")
    panel_rows = z.shape[0] // lax.axis_size("sub")
    panel = lax.dynamic_slice_in_dim(z, me * panel_rows, panel_rows, axis=0)
    return (panel, rotated, new_codebook)


def solution(mesh):
    in_specs = (P(("rows", "sub"), None), P(None, ("rows", "sub")), P(None, "sub"))
    out_specs = (P("sub", None), P(("rows", "sub"), None), P(None, "sub"))
    return jax.shard_map(body, mesh=mesh, in_specs=in_specs, out_specs=out_specs, check_vma=False)
```

```python
import jax
import jax.numpy as jnp
from jax import lax
from jax.sharding import PartitionSpec as P

NS_STEPS = 3


coef_a = 3.4445
coef_b = -4.775
coef_c = 2.0315
frob_eps = 1e-07


def one_hot_codes(code_block, count_codes):
    levels = lax.broadcasted_iota(jnp.int32, code_block.shape + (count_codes,), 2)
    return (code_block[:, :, None] == levels).astype(jnp.bfloat16)


def decode_rows(codes, table):
    subspaces, local_rows = codes.shape
    count_codes, row_width = table.shape
    sub_width = row_width // subspaces
    codewords = table.reshape(count_codes, subspaces, sub_width)
    one_hot = one_hot_codes(codes, count_codes)
    picked = jnp.einsum("mnk,kmj->nmj", one_hot, codewords, preferred_element_type=jnp.float32)
    return picked.reshape(local_rows, row_width).astype(jnp.bfloat16)


def codeword_totals(codes, row_values, count_codes):
    subspaces, local_rows = codes.shape
    row_width = row_values.shape[1]
    sub_width = row_width // subspaces
    one_hot = one_hot_codes(codes, count_codes)
    pieces = row_values.reshape(local_rows, subspaces, sub_width)
    code_sums = jnp.einsum("mnk,nmj->kmj", one_hot, pieces, preferred_element_type=jnp.float32)
    counts = jnp.sum(one_hot, axis=1, dtype=jnp.float32).T
    return code_sums.reshape(count_codes, row_width), counts


def rows_sum(x):
    groups = lax.axis_size("rows")
    chunk = x.shape[0] // groups
    scattered = lax.all_to_all(x, "rows", split_axis=0, concat_axis=0, tiled=True)
    own = jnp.sum(scattered.reshape((groups, chunk) + x.shape[1:]), axis=0)
    spread = jnp.broadcast_to(own[None], (groups,) + own.shape).reshape(x.shape)
    return lax.all_to_all(spread, "rows", split_axis=0, concat_axis=0, tiled=True)


def bdot(left, right, dims):
    return lax.dot_general(
        left.astype(jnp.bfloat16), right.astype(jnp.bfloat16), (dims, ((), ())),
        preferred_element_type=jnp.float32,
    )


def partner(x):
    count = lax.axis_size("sub")
    return lax.ppermute(x, "sub", [(i, i ^ 1) for i in range(count)])


def newton_half(z_own, z_other_half):
    own_half = z_own.astype(jnp.bfloat16)
    gram_own = bdot(own_half, own_half, ((1,), (1,)))
    gram_cross = bdot(own_half, z_other_half, ((1,), (1,)))
    gram_other = partner(gram_own.astype(jnp.bfloat16))
    own_block, cross_block = gram_own.astype(jnp.bfloat16), gram_cross.astype(jnp.bfloat16)
    quartic_left = bdot(own_block, own_block, ((1,), (0,))) + bdot(cross_block, cross_block, ((1,), (1,)))
    quartic_right = bdot(own_block, cross_block, ((1,), (0,))) + bdot(cross_block, gram_other, ((1,), (0,)))
    mixer_left = coef_b * gram_own + coef_c * quartic_left
    mixer_right = coef_b * gram_cross + coef_c * quartic_right
    return (
        coef_a * z_own
        + bdot(mixer_left, own_half, ((1,), (0,)))
        + bdot(mixer_right, z_other_half, ((1,), (0,)))
    )


def body(embeddings, codes, codebook):
    moved_codes = lax.all_to_all(codes, "sub", split_axis=0, concat_axis=1, tiled=True)
    groups = lax.axis_size("sub")
    copies = jnp.broadcast_to(codebook[None], (groups,) + codebook.shape)
    shards = lax.all_to_all(copies, "sub", split_axis=0, concat_axis=0, tiled=True)
    table = jnp.transpose(shards, (1, 0, 2)).reshape(codebook.shape[0], groups * codebook.shape[1])
    decoded = decode_rows(codes, table)
    partial = lax.dot_general(
        embeddings, decoded, (((0,), (0,)), ((), ())), preferred_element_type=jnp.float32
    )
    partial_panel = lax.psum_scatter(partial, "sub", scatter_dimension=0, tiled=True)
    cross_panel = rows_sum(partial_panel)
    cross = lax.all_gather(cross_panel, "sub", axis=0, tiled=True)
    frob_scale = jnp.sqrt(jnp.sum(cross * cross)) + frob_eps
    z = cross / frob_scale
    core = lax.axis_index("sub") % 2
    panel_rows = z.shape[0] // lax.axis_size("sub")
    by_parity = z.reshape(-1, 2, panel_rows, z.shape[1])
    z_own = lax.dynamic_index_in_dim(by_parity, core, axis=1, keepdims=False).reshape(-1, z.shape[1])
    z_other = lax.dynamic_index_in_dim(by_parity, 1 - core, axis=1, keepdims=False).reshape(-1, z.shape[1])
    z_other_half = z_other.astype(jnp.bfloat16)
    for newton_step_index in range(NS_STEPS):
        z_own = newton_half(z_own, z_other_half)
        z_other_half = partner(z_own.astype(jnp.bfloat16))
    own_panels = z_own.astype(jnp.bfloat16).reshape(-1, panel_rows, z.shape[1])
    other_panels = z_other_half.reshape(-1, panel_rows, z.shape[1])
    rotation_half = jnp.where(
        core == 0,
        jnp.stack([own_panels, other_panels], axis=1),
        jnp.stack([other_panels, own_panels], axis=1),
    ).reshape(z.shape)
    rotated = jnp.dot(embeddings, rotation_half, preferred_element_type=jnp.float32).astype(
        jnp.bfloat16
    )
    moved_rows = lax.all_to_all(rotated, "sub", split_axis=1, concat_axis=0, tiled=True)
    code_sums, counts = codeword_totals(moved_codes, moved_rows, table.shape[0])
    sums_width = code_sums.shape[1]
    totals = rows_sum(jnp.concatenate([code_sums, counts], axis=1))
    code_sums, counts = totals[:, :sums_width], totals[:, sums_width:]
    own_codebook = codebook.astype(jnp.float32)
    spread = jnp.repeat(counts, own_codebook.shape[1] // counts.shape[1], axis=1)
    new_codebook = (code_sums + own_codebook) / (spread + 1.0)
    me = lax.axis_index("sub")
    panel = lax.dynamic_index_in_dim(z_own.reshape(-1, panel_rows, z.shape[1]), me // 2, axis=0, keepdims=False)
    return (panel, rotated, new_codebook)


def solution(mesh):
    in_specs = (P(("rows", "sub"), None), P(None, ("rows", "sub")), P(None, "sub"))
    out_specs = (P("sub", None), P(("rows", "sub"), None), P(None, "sub"))
    return jax.shard_map(body, mesh=mesh, in_specs=in_specs, out_specs=out_specs, check_vma=False)
```

```python
import jax
import jax.numpy as jnp
from jax import lax
from jax.sharding import PartitionSpec as P

NS_STEPS = 3


coef_a = 3.4445
coef_b = -4.775
coef_c = 2.0315
frob_eps = 1e-07


def one_hot_codes(code_block, count_codes):
    levels = lax.broadcasted_iota(jnp.int32, code_block.shape + (count_codes,), 2)
    return (code_block[:, :, None] == levels).astype(jnp.bfloat16)


def decode_rows(codes, table):
    subspaces, local_rows = codes.shape
    count_codes, row_width = table.shape
    sub_width = row_width // subspaces
    codewords = table.reshape(count_codes, subspaces, sub_width)
    one_hot = one_hot_codes(codes, count_codes)
    picked = jnp.einsum("mnk,kmj->nmj", one_hot, codewords, preferred_element_type=jnp.float32)
    return picked.reshape(local_rows, row_width).astype(jnp.bfloat16)


def codeword_sums(codes, row_values, count_codes):
    subspaces, local_rows = codes.shape
    row_width = row_values.shape[1]
    sub_width = row_width // subspaces
    one_hot = one_hot_codes(codes, count_codes)
    pieces = row_values.reshape(local_rows, subspaces, sub_width)
    code_sums = jnp.einsum("mnk,nmj->kmj", one_hot, pieces, preferred_element_type=jnp.float32)
    return code_sums.reshape(count_codes, row_width)


def rows_sum(x):
    groups = lax.axis_size("rows")
    chunk = x.shape[0] // groups
    scattered = lax.all_to_all(x, "rows", split_axis=0, concat_axis=0, tiled=True)
    own = jnp.sum(scattered.reshape((groups, chunk) + x.shape[1:]), axis=0)
    spread = jnp.broadcast_to(own[None], (groups,) + own.shape).reshape(x.shape)
    return lax.all_to_all(spread, "rows", split_axis=0, concat_axis=0, tiled=True)


def bdot(left, right, dims):
    return lax.dot_general(
        left.astype(jnp.bfloat16), right.astype(jnp.bfloat16), (dims, ((), ())),
        preferred_element_type=jnp.float32,
    )


def partner(x):
    count = lax.axis_size("sub")
    return lax.ppermute(x, "sub", [(i, i ^ 1) for i in range(count)])


def newton_half(z_own, z_other_half):
    own_half = z_own.astype(jnp.bfloat16)
    gram_own = bdot(own_half, own_half, ((1,), (1,)))
    gram_cross = bdot(own_half, z_other_half, ((1,), (1,)))
    gram_other = partner(gram_own.astype(jnp.bfloat16))
    own_block, cross_block = gram_own.astype(jnp.bfloat16), gram_cross.astype(jnp.bfloat16)
    quartic_left = bdot(own_block, own_block, ((1,), (0,))) + bdot(cross_block, cross_block, ((1,), (1,)))
    quartic_right = bdot(own_block, cross_block, ((1,), (0,))) + bdot(cross_block, gram_other, ((1,), (0,)))
    mixer_left = coef_b * gram_own + coef_c * quartic_left
    mixer_right = coef_b * gram_cross + coef_c * quartic_right
    return (
        coef_a * z_own
        + bdot(mixer_left, own_half, ((1,), (0,)))
        + bdot(mixer_right, z_other_half, ((1,), (0,)))
    )


def body(embeddings, codes, codebook):
    moved_codes = lax.all_to_all(codes, "sub", split_axis=0, concat_axis=1, tiled=True)
    table = lax.all_gather(codebook, "sub", axis=1, tiled=True)
    decoded = decode_rows(codes, table)
    partial_t = lax.dot_general(
        decoded, embeddings, (((0,), (0,)), ((), ())), preferred_element_type=jnp.float32
    )
    partial_panel = lax.psum_scatter(partial_t, "sub", scatter_dimension=1, tiled=True).T
    code_one_hot = one_hot_codes(moved_codes, table.shape[0])
    counts = jnp.sum(code_one_hot, axis=1, dtype=jnp.float32).T
    partial_panel, moved_codes, counts = lax.optimization_barrier((partial_panel, moved_codes, counts))
    cross_panel = rows_sum(partial_panel)
    cross = lax.all_gather(cross_panel, "sub", axis=0, tiled=True)
    frob_scale = jnp.sqrt(jnp.sum(cross * cross)) + frob_eps
    z = cross / frob_scale
    core = lax.axis_index("sub") % 2
    panel_rows = z.shape[0] // lax.axis_size("sub")
    by_parity = z.reshape(-1, 2, panel_rows, z.shape[1])
    z_own = lax.dynamic_index_in_dim(by_parity, core, axis=1, keepdims=False).reshape(-1, z.shape[1])
    z_other = lax.dynamic_index_in_dim(by_parity, 1 - core, axis=1, keepdims=False).reshape(-1, z.shape[1])
    z_other_half = z_other.astype(jnp.bfloat16)
    for newton_step_index in range(NS_STEPS):
        z_own = newton_half(z_own, z_other_half)
        z_other_half = partner(z_own.astype(jnp.bfloat16))
    own_panels = z_own.astype(jnp.bfloat16).reshape(-1, panel_rows, z.shape[1])
    other_panels = z_other_half.reshape(-1, panel_rows, z.shape[1])
    rotation_half = jnp.where(
        core == 0,
        jnp.stack([own_panels, other_panels], axis=1),
        jnp.stack([other_panels, own_panels], axis=1),
    ).reshape(z.shape)
    rotated = jnp.dot(embeddings, rotation_half, preferred_element_type=jnp.float32).astype(
        jnp.bfloat16
    )
    moved_rows = lax.all_to_all(rotated, "sub", split_axis=1, concat_axis=0, tiled=True)
    code_sums = codeword_sums(moved_codes, moved_rows, table.shape[0])
    sums_width = code_sums.shape[1]
    totals = rows_sum(jnp.concatenate([code_sums, counts], axis=1))
    code_sums, counts = totals[:, :sums_width], totals[:, sums_width:]
    own_codebook = codebook.astype(jnp.float32)
    spread = jnp.repeat(counts, own_codebook.shape[1] // counts.shape[1], axis=1)
    new_codebook = (code_sums + own_codebook) / (spread + 1.0)
    me = lax.axis_index("sub")
    panel = lax.dynamic_index_in_dim(z_own.reshape(-1, panel_rows, z.shape[1]), me // 2, axis=0, keepdims=False)
    return (panel, rotated, new_codebook)


def solution(mesh):
    in_specs = (P(("rows", "sub"), None), P(None, ("rows", "sub")), P(None, "sub"))
    out_specs = (P("sub", None), P(("rows", "sub"), None), P(None, "sub"))
    return jax.shard_map(body, mesh=mesh, in_specs=in_specs, out_specs=out_specs, check_vma=False)
```

```python
import jax
import jax.numpy as jnp
from jax import lax
from jax.sharding import PartitionSpec as P

NS_STEPS = 3


coef_a = 3.4445
coef_b = -4.775
coef_c = 2.0315
frob_eps = 1e-07


def one_hot_codes(code_block, count_codes):
    levels = lax.broadcasted_iota(jnp.int32, code_block.shape + (count_codes,), 2)
    return (code_block[:, :, None] == levels).astype(jnp.bfloat16)


def decode_rows(codes, table):
    subspaces, local_rows = codes.shape
    count_codes, row_width = table.shape
    sub_width = row_width // subspaces
    codewords = table.reshape(count_codes, subspaces, sub_width)
    one_hot = one_hot_codes(codes, count_codes)
    picked = jnp.einsum("mnk,kmj->nmj", one_hot, codewords, preferred_element_type=jnp.float32)
    return picked.reshape(local_rows, row_width).astype(jnp.bfloat16)


def codeword_sums(codes, row_values, count_codes):
    subspaces, local_rows = codes.shape
    row_width = row_values.shape[1]
    sub_width = row_width // subspaces
    one_hot = one_hot_codes(codes, count_codes)
    pieces = row_values.reshape(local_rows, subspaces, sub_width)
    code_sums = jnp.einsum("mnk,nmj->kmj", one_hot, pieces, preferred_element_type=jnp.float32)
    return code_sums.reshape(count_codes, row_width)


def rows_sum(x):
    groups = lax.axis_size("rows")
    chunk = x.shape[0] // groups
    scattered = lax.all_to_all(x, "rows", split_axis=0, concat_axis=0, tiled=True)
    own = jnp.sum(scattered.reshape((groups, chunk) + x.shape[1:]), axis=0)
    spread = jnp.broadcast_to(own[None], (groups,) + own.shape).reshape(x.shape)
    return lax.all_to_all(spread, "rows", split_axis=0, concat_axis=0, tiled=True)


def bdot(left, right, dims):
    return lax.dot_general(
        left.astype(jnp.bfloat16), right.astype(jnp.bfloat16), (dims, ((), ())),
        preferred_element_type=jnp.float32,
    )


def partner(x):
    count = lax.axis_size("sub")
    return lax.ppermute(x, "sub", [(i, i ^ 1) for i in range(count)])


def newton_half(z_own, z_other_half):
    own_half = z_own.astype(jnp.bfloat16)
    gram_own = bdot(own_half, own_half, ((1,), (1,)))
    gram_cross = bdot(own_half, z_other_half, ((1,), (1,)))
    gram_other = partner(gram_own.astype(jnp.bfloat16))
    own_block, cross_block = gram_own.astype(jnp.bfloat16), gram_cross.astype(jnp.bfloat16)
    quartic_left = bdot(own_block, own_block, ((1,), (0,))) + bdot(cross_block, cross_block, ((1,), (1,)))
    quartic_right = bdot(own_block, cross_block, ((1,), (0,))) + bdot(cross_block, gram_other, ((1,), (0,)))
    mixer_left = coef_b * gram_own + coef_c * quartic_left
    mixer_right = coef_b * gram_cross + coef_c * quartic_right
    return (
        coef_a * z_own
        + bdot(mixer_left, own_half, ((1,), (0,)))
        + bdot(mixer_right, z_other_half, ((1,), (0,)))
    )


def body(embeddings, codes, codebook):
    moved_codes = lax.all_to_all(codes, "sub", split_axis=0, concat_axis=1, tiled=True)
    table = lax.all_gather(codebook, "sub", axis=1, tiled=True)
    decoded = decode_rows(codes, table)
    partial_t = lax.dot_general(
        decoded, embeddings, (((0,), (0,)), ((), ())), preferred_element_type=jnp.float32
    )
    partial_panel = lax.psum_scatter(partial_t, "sub", scatter_dimension=1, tiled=True).T
    code_one_hot = one_hot_codes(moved_codes, table.shape[0])
    counts = jnp.sum(code_one_hot, axis=1, dtype=jnp.float32).T
    partial_panel, moved_codes, counts = lax.optimization_barrier((partial_panel, moved_codes, counts))
    cross_panel = rows_sum(partial_panel)
    panel_rows, width = cross_panel.shape
    squares = jnp.broadcast_to(jnp.sum(cross_panel * cross_panel), (8, width))
    gathered = lax.all_gather(jnp.concatenate([cross_panel, squares], axis=0), "sub", axis=0, tiled=True)
    gathered = gathered.reshape(-1, panel_rows + 8, width)
    frob_scale = jnp.sqrt(jnp.sum(gathered[:, panel_rows, 0])) + frob_eps
    core = lax.axis_index("sub") % 2
    by_parity = gathered.reshape(-1, 2, panel_rows + 8, width)
    own_rows = lax.dynamic_index_in_dim(by_parity, core, axis=1, keepdims=False)
    other_rows = lax.dynamic_index_in_dim(by_parity, 1 - core, axis=1, keepdims=False)
    z_own = own_rows[:, :panel_rows, :].reshape(-1, width) / frob_scale
    z_other = other_rows[:, :panel_rows, :].reshape(-1, width) / frob_scale
    z_other_half = z_other.astype(jnp.bfloat16)
    for newton_step_index in range(NS_STEPS):
        z_own = newton_half(z_own, z_other_half)
        z_other_half = partner(z_own.astype(jnp.bfloat16))
    own_panels = z_own.astype(jnp.bfloat16).reshape(-1, panel_rows, width)
    other_panels = z_other_half.reshape(-1, panel_rows, width)
    rotation_half = jnp.where(
        core == 0,
        jnp.stack([own_panels, other_panels], axis=1),
        jnp.stack([other_panels, own_panels], axis=1),
    ).reshape(-1, width)
    rotated = jnp.dot(embeddings, rotation_half, preferred_element_type=jnp.float32).astype(
        jnp.bfloat16
    )
    moved_rows = lax.all_to_all(rotated, "sub", split_axis=1, concat_axis=0, tiled=True)
    code_sums = codeword_sums(moved_codes, moved_rows, table.shape[0])
    sums_width = code_sums.shape[1]
    totals = rows_sum(jnp.concatenate([code_sums, counts], axis=1))
    code_sums, counts = totals[:, :sums_width], totals[:, sums_width:]
    own_codebook = codebook.astype(jnp.float32)
    spread = jnp.repeat(counts, own_codebook.shape[1] // counts.shape[1], axis=1)
    new_codebook = (code_sums + own_codebook) / (spread + 1.0)
    me = lax.axis_index("sub")
    panel = lax.dynamic_index_in_dim(z_own.reshape(-1, panel_rows, width), me // 2, axis=0, keepdims=False)
    return (panel, rotated, new_codebook)


def solution(mesh):
    in_specs = (P(("rows", "sub"), None), P(None, ("rows", "sub")), P(None, "sub"))
    out_specs = (P("sub", None), P(("rows", "sub"), None), P(None, "sub"))
    return jax.shard_map(body, mesh=mesh, in_specs=in_specs, out_specs=out_specs, check_vma=False)
```

```python
import jax
import jax.numpy as jnp
from jax import lax
from jax.sharding import PartitionSpec as P

NS_STEPS = 3


coef_a = 3.4445
coef_b = -4.775
coef_c = 2.0315
frob_eps = 1e-07


def one_hot_codes(code_block, count_codes):
    levels = lax.broadcasted_iota(jnp.int32, code_block.shape + (count_codes,), 2)
    return (code_block[:, :, None] == levels).astype(jnp.bfloat16)


def decode_rows(codes, table):
    subspaces, local_rows = codes.shape
    count_codes, row_width = table.shape
    sub_width = row_width // subspaces
    codewords = table.reshape(count_codes, subspaces, sub_width)
    one_hot = one_hot_codes(codes, count_codes)
    picked = jnp.einsum("mnk,kmj->nmj", one_hot, codewords, preferred_element_type=jnp.float32)
    return picked.reshape(local_rows, row_width).astype(jnp.bfloat16)


def codeword_sums(codes, row_values, count_codes):
    subspaces, local_rows = codes.shape
    row_width = row_values.shape[1]
    sub_width = row_width // subspaces
    one_hot = one_hot_codes(codes, count_codes)
    pieces = row_values.reshape(local_rows, subspaces, sub_width)
    code_sums = jnp.einsum("mnk,nmj->kmj", one_hot, pieces, preferred_element_type=jnp.float32)
    return code_sums.reshape(count_codes, row_width)


def rows_sum(x):
    groups = lax.axis_size("rows")
    chunk = x.shape[0] // groups
    scattered = lax.all_to_all(x, "rows", split_axis=0, concat_axis=0, tiled=True)
    own = jnp.sum(scattered.reshape((groups, chunk) + x.shape[1:]), axis=0)
    spread = jnp.broadcast_to(own[None], (groups,) + own.shape).reshape(x.shape)
    return lax.all_to_all(spread, "rows", split_axis=0, concat_axis=0, tiled=True)


def bdot(left, right, dims):
    return lax.dot_general(
        left.astype(jnp.bfloat16), right.astype(jnp.bfloat16), (dims, ((), ())),
        preferred_element_type=jnp.float32,
    )


def partner(x):
    count = lax.axis_size("sub")
    return lax.ppermute(x, "sub", [(i, i ^ 1) for i in range(count)])


def newton_half(z_own, z_other_half):
    own_half = z_own.astype(jnp.bfloat16)
    gram_own = bdot(own_half, own_half, ((1,), (1,)))
    gram_cross = bdot(own_half, z_other_half, ((1,), (1,)))
    gram_other = partner(gram_own.astype(jnp.bfloat16))
    own_block, cross_block = gram_own.astype(jnp.bfloat16), gram_cross.astype(jnp.bfloat16)
    gram_rows = jnp.concatenate([own_block, cross_block], axis=1)
    quartic_left = bdot(gram_rows, gram_rows, ((1,), (1,)))
    quartic_right = bdot(own_block, cross_block, ((1,), (0,))) + bdot(cross_block, gram_other, ((1,), (0,)))
    mixer = jnp.concatenate(
        [coef_b * gram_own + coef_c * quartic_left, coef_b * gram_cross + coef_c * quartic_right], axis=1
    )
    local_rows = jnp.concatenate([own_half, z_other_half], axis=0)
    return coef_a * z_own + bdot(mixer, local_rows, ((1,), (0,)))


def body(embeddings, codes, codebook):
    moved_codes = lax.all_to_all(codes, "sub", split_axis=0, concat_axis=1, tiled=True)
    table = lax.all_gather(codebook, "sub", axis=1, tiled=True)
    decoded = decode_rows(codes, table)
    partial_t = lax.dot_general(
        decoded, embeddings, (((0,), (0,)), ((), ())), preferred_element_type=jnp.float32
    )
    partial_panel = lax.psum_scatter(partial_t, "sub", scatter_dimension=1, tiled=True).T
    code_one_hot = one_hot_codes(moved_codes, table.shape[0])
    counts = jnp.sum(code_one_hot, axis=1, dtype=jnp.float32).T
    partial_panel, moved_codes, counts = lax.optimization_barrier((partial_panel, moved_codes, counts))
    cross_panel = rows_sum(partial_panel)
    cross = lax.all_gather(cross_panel, "sub", axis=0, tiled=True)
    frob_scale = jnp.sqrt(jnp.sum(cross * cross)) + frob_eps
    z = cross / frob_scale
    core = lax.axis_index("sub") % 2
    panel_rows = z.shape[0] // lax.axis_size("sub")
    by_parity = z.reshape(-1, 2, panel_rows, z.shape[1])
    z_own = lax.dynamic_index_in_dim(by_parity, core, axis=1, keepdims=False).reshape(-1, z.shape[1])
    z_other = lax.dynamic_index_in_dim(by_parity, 1 - core, axis=1, keepdims=False).reshape(-1, z.shape[1])
    z_other_half = z_other.astype(jnp.bfloat16)
    for newton_step_index in range(NS_STEPS):
        z_own = newton_half(z_own, z_other_half)
        z_other_half = partner(z_own.astype(jnp.bfloat16))
    own_panels = z_own.astype(jnp.bfloat16).reshape(-1, panel_rows, z.shape[1])
    other_panels = z_other_half.reshape(-1, panel_rows, z.shape[1])
    rotation_half = jnp.where(
        core == 0,
        jnp.stack([own_panels, other_panels], axis=1),
        jnp.stack([other_panels, own_panels], axis=1),
    ).reshape(z.shape)
    rotated = jnp.dot(embeddings, rotation_half, preferred_element_type=jnp.float32).astype(
        jnp.bfloat16
    )
    moved_rows = lax.all_to_all(rotated, "sub", split_axis=1, concat_axis=0, tiled=True)
    code_sums = codeword_sums(moved_codes, moved_rows, table.shape[0])
    sums_width = code_sums.shape[1]
    totals = rows_sum(jnp.concatenate([code_sums, counts], axis=1))
    code_sums, counts = totals[:, :sums_width], totals[:, sums_width:]
    own_codebook = codebook.astype(jnp.float32)
    spread = jnp.repeat(counts, own_codebook.shape[1] // counts.shape[1], axis=1)
    new_codebook = (code_sums + own_codebook) / (spread + 1.0)
    me = lax.axis_index("sub")
    panel = lax.dynamic_index_in_dim(z_own.reshape(-1, panel_rows, z.shape[1]), me // 2, axis=0, keepdims=False)
    return (panel, rotated, new_codebook)


def solution(mesh):
    in_specs = (P(("rows", "sub"), None), P(None, ("rows", "sub")), P(None, "sub"))
    out_specs = (P("sub", None), P(("rows", "sub"), None), P(None, "sub"))
    return jax.shard_map(body, mesh=mesh, in_specs=in_specs, out_specs=out_specs, check_vma=False)
```

```python
import jax
import jax.numpy as jnp
from jax import lax
from jax.sharding import PartitionSpec as P

NS_STEPS = 3


coef_a = 3.4445
coef_b = -4.775
coef_c = 2.0315
frob_eps = 1e-07


def one_hot_codes(code_block, count_codes):
    levels = lax.broadcasted_iota(jnp.int32, code_block.shape + (count_codes,), 2)
    return (code_block[:, :, None] == levels).astype(jnp.bfloat16)


def decode_rows(codes, table):
    subspaces, local_rows = codes.shape
    count_codes, row_width = table.shape
    sub_width = row_width // subspaces
    codewords = table.reshape(count_codes, subspaces, sub_width)
    one_hot = one_hot_codes(codes, count_codes)
    picked = jnp.einsum("mnk,kmj->nmj", one_hot, codewords, preferred_element_type=jnp.float32)
    return picked.reshape(local_rows, row_width).astype(jnp.bfloat16)


def codeword_sums(codes, row_values, count_codes):
    subspaces, local_rows = codes.shape
    row_width = row_values.shape[1]
    sub_width = row_width // subspaces
    one_hot = one_hot_codes(codes, count_codes)
    pieces = row_values.reshape(local_rows, subspaces, sub_width)
    code_sums = jnp.einsum("mnk,nmj->kmj", one_hot, pieces, preferred_element_type=jnp.float32)
    return code_sums.reshape(count_codes, row_width)


def rows_sum(x):
    groups = lax.axis_size("rows")
    chunk = x.shape[0] // groups
    scattered = lax.all_to_all(x, "rows", split_axis=0, concat_axis=0, tiled=True)
    own = jnp.sum(scattered.reshape((groups, chunk) + x.shape[1:]), axis=0)
    spread = jnp.broadcast_to(own[None], (groups,) + own.shape).reshape(x.shape)
    return lax.all_to_all(spread, "rows", split_axis=0, concat_axis=0, tiled=True)


def bdot(left, right, dims):
    return lax.dot_general(
        left.astype(jnp.bfloat16), right.astype(jnp.bfloat16), (dims, ((), ())),
        preferred_element_type=jnp.float32,
    )


def partner(x):
    count = lax.axis_size("sub")
    return lax.ppermute(x, "sub", [(i, i ^ 1) for i in range(count)])


def newton_half(z_own, z_other_half):
    own_half = z_own.astype(jnp.bfloat16)
    gram_own = bdot(own_half, own_half, ((1,), (1,)))
    gram_cross = bdot(own_half, z_other_half, ((1,), (1,)))
    gram_other = partner(gram_own.astype(jnp.bfloat16))
    own_block, cross_block = gram_own.astype(jnp.bfloat16), gram_cross.astype(jnp.bfloat16)
    gram_rows = jnp.concatenate([own_block, cross_block], axis=1)
    quartic_left = bdot(gram_rows, gram_rows, ((1,), (1,)))
    quartic_right = bdot(own_block, cross_block, ((1,), (0,))) + bdot(cross_block, gram_other, ((1,), (0,)))
    mixer = jnp.concatenate(
        [coef_b * gram_own + coef_c * quartic_left, coef_b * gram_cross + coef_c * quartic_right], axis=1
    )
    local_rows = jnp.concatenate([own_half, z_other_half], axis=0)
    return coef_a * z_own + bdot(mixer, local_rows, ((1,), (0,)))


def body(embeddings, codes, codebook):
    moved_codes = lax.all_to_all(codes, "sub", split_axis=0, concat_axis=1, tiled=True)
    table = lax.all_gather(codebook, "sub", axis=1, tiled=True)
    decoded = decode_rows(codes, table)
    partial_t = lax.dot_general(
        decoded, embeddings, (((0,), (0,)), ((), ())), preferred_element_type=jnp.float32
    )
    partial_panel = lax.psum_scatter(partial_t, "sub", scatter_dimension=1, tiled=True).T
    code_one_hot = one_hot_codes(moved_codes, table.shape[0])
    counts = jnp.sum(code_one_hot, axis=1, dtype=jnp.float32).T
    partial_panel, moved_codes, counts = lax.optimization_barrier((partial_panel, moved_codes, counts))
    cross_panel = rows_sum(partial_panel)
    cross = lax.all_gather(cross_panel, "sub", axis=0, tiled=True)
    width = cross.shape[1]
    square_rows = jnp.sum((cross * cross).reshape(-1, 8, width), axis=1)
    frob_scale = jnp.sqrt(jnp.sum(lax.optimization_barrier(square_rows))) + frob_eps
    core = lax.axis_index("sub") % 2
    panel_rows = cross.shape[0] // lax.axis_size("sub")
    by_parity = cross.reshape(-1, 2, panel_rows, width)
    z_own = lax.dynamic_index_in_dim(by_parity, core, axis=1, keepdims=False).reshape(-1, width) / frob_scale
    z_other = lax.dynamic_index_in_dim(by_parity, 1 - core, axis=1, keepdims=False).reshape(-1, width) / frob_scale
    z_other_half = z_other.astype(jnp.bfloat16)
    for newton_step_index in range(NS_STEPS):
        z_own = newton_half(z_own, z_other_half)
        z_other_half = partner(z_own.astype(jnp.bfloat16))
    own_panels = z_own.astype(jnp.bfloat16).reshape(-1, panel_rows, width)
    other_panels = z_other_half.reshape(-1, panel_rows, width)
    rotation_half = jnp.where(
        core == 0,
        jnp.stack([own_panels, other_panels], axis=1),
        jnp.stack([other_panels, own_panels], axis=1),
    ).reshape(-1, width)
    rotated = jnp.dot(embeddings, rotation_half, preferred_element_type=jnp.float32).astype(
        jnp.bfloat16
    )
    moved_rows = lax.all_to_all(rotated, "sub", split_axis=1, concat_axis=0, tiled=True)
    code_sums = codeword_sums(moved_codes, moved_rows, table.shape[0])
    sums_width = code_sums.shape[1]
    totals = rows_sum(jnp.concatenate([code_sums, counts], axis=1))
    code_sums, counts = totals[:, :sums_width], totals[:, sums_width:]
    own_codebook = codebook.astype(jnp.float32)
    spread = jnp.repeat(counts, own_codebook.shape[1] // counts.shape[1], axis=1)
    new_codebook = (code_sums + own_codebook) / (spread + 1.0)
    me = lax.axis_index("sub")
    panel = lax.dynamic_index_in_dim(z_own.reshape(-1, panel_rows, width), me // 2, axis=0, keepdims=False)
    return (panel, rotated, new_codebook)


def solution(mesh):
    in_specs = (P(("rows", "sub"), None), P(None, ("rows", "sub")), P(None, "sub"))
    out_specs = (P("sub", None), P(("rows", "sub"), None), P(None, "sub"))
    return jax.shard_map(body, mesh=mesh, in_specs=in_specs, out_specs=out_specs, check_vma=False)
```

```python
import jax
import jax.numpy as jnp
from jax import lax
from jax.sharding import PartitionSpec as P

NS_STEPS = 3


coef_a = 3.4445
coef_b = -4.775
coef_c = 2.0315
frob_eps = 1e-07


def one_hot_codes(code_block, count_codes):
    levels = lax.broadcasted_iota(jnp.int32, code_block.shape + (count_codes,), 2)
    return (code_block[:, :, None] == levels).astype(jnp.bfloat16)


def decode_rows(codes, table):
    subspaces, local_rows = codes.shape
    count_codes, row_width = table.shape
    sub_width = row_width // subspaces
    codewords = table.reshape(count_codes, subspaces, sub_width)
    one_hot = one_hot_codes(codes, count_codes)
    picked = jnp.einsum("mnk,kmj->nmj", one_hot, codewords, preferred_element_type=jnp.float32)
    return picked.reshape(local_rows, row_width).astype(jnp.bfloat16)


def codeword_sums(codes, row_values, count_codes):
    subspaces, local_rows = codes.shape
    row_width = row_values.shape[1]
    sub_width = row_width // subspaces
    one_hot = one_hot_codes(codes, count_codes)
    pieces = row_values.reshape(local_rows, subspaces, sub_width)
    code_sums = jnp.einsum("mnk,nmj->kmj", one_hot, pieces, preferred_element_type=jnp.float32)
    return code_sums.reshape(count_codes, row_width)


def rows_sum(x):
    groups = lax.axis_size("rows")
    chunk = x.shape[0] // groups
    scattered = lax.all_to_all(x, "rows", split_axis=0, concat_axis=0, tiled=True)
    own = jnp.sum(scattered.reshape((groups, chunk) + x.shape[1:]), axis=0)
    spread = jnp.broadcast_to(own[None], (groups,) + own.shape).reshape(x.shape)
    return lax.all_to_all(spread, "rows", split_axis=0, concat_axis=0, tiled=True)


def bdot(left, right, dims):
    return lax.dot_general(
        left.astype(jnp.bfloat16), right.astype(jnp.bfloat16), (dims, ((), ())),
        preferred_element_type=jnp.float32,
    )


def partner(x):
    count = lax.axis_size("sub")
    return lax.ppermute(x, "sub", [(i, i ^ 1) for i in range(count)])


def newton_half(z_own, z_other_half):
    own_half = z_own.astype(jnp.bfloat16)
    gram_own = bdot(own_half, own_half, ((1,), (1,)))
    gram_cross = bdot(own_half, z_other_half, ((1,), (1,)))
    gram_other = partner(gram_own.astype(jnp.bfloat16))
    own_block, cross_block = gram_own.astype(jnp.bfloat16), gram_cross.astype(jnp.bfloat16)
    gram_rows = jnp.concatenate([own_block, cross_block], axis=1)
    quartic_left = bdot(gram_rows, gram_rows, ((1,), (1,)))
    quartic_right = bdot(own_block, cross_block, ((1,), (0,))) + bdot(cross_block, gram_other, ((1,), (0,)))
    mixer = jnp.concatenate(
        [coef_b * gram_own + coef_c * quartic_left, coef_b * gram_cross + coef_c * quartic_right], axis=1
    )
    local_rows = jnp.concatenate([own_half, z_other_half], axis=0)
    return coef_a * z_own + bdot(mixer, local_rows, ((1,), (0,)))


def body(embeddings, codes, codebook):
    moved_codes = lax.all_to_all(codes, "sub", split_axis=0, concat_axis=1, tiled=True)
    table = lax.all_gather(codebook, "sub", axis=1, tiled=True)
    decoded = decode_rows(codes, table)
    partial_t = lax.dot_general(
        decoded, embeddings, (((0,), (0,)), ((), ())), preferred_element_type=jnp.float32
    )
    partial_panel = lax.psum_scatter(partial_t, "sub", scatter_dimension=1, tiled=True).T
    code_one_hot = one_hot_codes(moved_codes, table.shape[0])
    counts = jnp.sum(code_one_hot, axis=1, dtype=jnp.float32).T
    partial_panel, moved_codes, counts = lax.optimization_barrier((partial_panel, moved_codes, counts))
    cross_panel = rows_sum(partial_panel)
    cross = lax.all_gather(cross_panel, "sub", axis=0, tiled=True)
    width = cross.shape[1]
    frob_scale = jnp.sqrt(jnp.sum(cross * cross)) + frob_eps
    core = lax.axis_index("sub") % 2
    panel_rows = cross.shape[0] // lax.axis_size("sub")
    by_parity = cross.reshape(-1, 2, panel_rows, width)
    z_own = lax.dynamic_index_in_dim(by_parity, core, axis=1, keepdims=False).reshape(-1, width) / frob_scale
    z_other = lax.dynamic_index_in_dim(by_parity, 1 - core, axis=1, keepdims=False).reshape(-1, width) / frob_scale
    z_other_half = z_other.astype(jnp.bfloat16)
    for newton_step_index in range(NS_STEPS - 1):
        z_own = newton_half(z_own, z_other_half)
        z_other_half = partner(z_own.astype(jnp.bfloat16))
    z_own = newton_half(z_own, z_other_half)
    own_half = z_own.astype(jnp.bfloat16)
    z_other_half = partner(own_half)
    columns = embeddings.reshape(embeddings.shape[0], -1, 2, panel_rows)
    own_columns = lax.dynamic_index_in_dim(columns, core, axis=2, keepdims=False).reshape(embeddings.shape[0], -1)
    other_columns = lax.dynamic_index_in_dim(columns, 1 - core, axis=2, keepdims=False).reshape(embeddings.shape[0], -1)
    rotated = (
        jnp.dot(own_columns, own_half, preferred_element_type=jnp.float32)
        + jnp.dot(other_columns, z_other_half, preferred_element_type=jnp.float32)
    ).astype(jnp.bfloat16)
    moved_rows = lax.all_to_all(rotated, "sub", split_axis=1, concat_axis=0, tiled=True)
    code_sums = codeword_sums(moved_codes, moved_rows, table.shape[0])
    sums_width = code_sums.shape[1]
    totals = rows_sum(jnp.concatenate([code_sums, counts], axis=1))
    code_sums, counts = totals[:, :sums_width], totals[:, sums_width:]
    own_codebook = codebook.astype(jnp.float32)
    spread = jnp.repeat(counts, own_codebook.shape[1] // counts.shape[1], axis=1)
    new_codebook = (code_sums + own_codebook) / (spread + 1.0)
    me = lax.axis_index("sub")
    panel = lax.dynamic_index_in_dim(z_own.reshape(-1, panel_rows, width), me // 2, axis=0, keepdims=False)
    return (panel, rotated, new_codebook)


def solution(mesh):
    in_specs = (P(("rows", "sub"), None), P(None, ("rows", "sub")), P(None, "sub"))
    out_specs = (P("sub", None), P(("rows", "sub"), None), P(None, "sub"))
    return jax.shard_map(body, mesh=mesh, in_specs=in_specs, out_specs=out_specs, check_vma=False)
```

```python
import jax
import jax.numpy as jnp
from jax import lax
from jax.sharding import PartitionSpec as P

NS_STEPS = 3


coef_a = 3.4445
coef_b = -4.775
coef_c = 2.0315
frob_eps = 1e-07


def one_hot_codes(code_block, count_codes):
    levels = lax.broadcasted_iota(jnp.int32, code_block.shape + (count_codes,), 2)
    return (code_block[:, :, None] == levels).astype(jnp.bfloat16)


def decode_rows(codes, table):
    subspaces, local_rows = codes.shape
    count_codes, row_width = table.shape
    sub_width = row_width // subspaces
    codewords = table.reshape(count_codes, subspaces, sub_width)
    one_hot = one_hot_codes(codes, count_codes)
    picked = jnp.einsum("mnk,kmj->nmj", one_hot, codewords, preferred_element_type=jnp.float32)
    return picked.reshape(local_rows, row_width).astype(jnp.bfloat16)


def codeword_sums(codes, row_values, count_codes):
    subspaces, local_rows = codes.shape
    row_width = row_values.shape[1]
    sub_width = row_width // subspaces
    one_hot = one_hot_codes(codes, count_codes)
    pieces = row_values.reshape(local_rows, subspaces, sub_width)
    code_sums = jnp.einsum("mnk,nmj->kmj", one_hot, pieces, preferred_element_type=jnp.float32)
    return code_sums.reshape(count_codes, row_width)


def rows_sum(x):
    groups = lax.axis_size("rows")
    chunk = x.shape[0] // groups
    scattered = lax.all_to_all(x, "rows", split_axis=0, concat_axis=0, tiled=True)
    own = jnp.sum(scattered.reshape((groups, chunk) + x.shape[1:]), axis=0)
    spread = jnp.broadcast_to(own[None], (groups,) + own.shape).reshape(x.shape)
    return lax.all_to_all(spread, "rows", split_axis=0, concat_axis=0, tiled=True)


def bdot(left, right, dims):
    return lax.dot_general(
        left.astype(jnp.bfloat16), right.astype(jnp.bfloat16), (dims, ((), ())),
        preferred_element_type=jnp.float32,
    )


def partner(x):
    count = lax.axis_size("sub")
    return lax.ppermute(x, "sub", [(i, i ^ 1) for i in range(count)])


def newton_half(z_own, z_other_half):
    own_half = z_own.astype(jnp.bfloat16)
    gram_own = bdot(own_half, own_half, ((1,), (1,)))
    gram_cross = bdot(own_half, z_other_half, ((1,), (1,)))
    gram_other = partner(gram_own.astype(jnp.bfloat16))
    own_block, cross_block = gram_own.astype(jnp.bfloat16), gram_cross.astype(jnp.bfloat16)
    gram_rows = jnp.concatenate([own_block, cross_block], axis=1)
    quartic_left = bdot(gram_rows, gram_rows, ((1,), (1,)))
    quartic_right = bdot(own_block, cross_block, ((1,), (0,))) + bdot(cross_block, gram_other, ((1,), (0,)))
    mixer = jnp.concatenate(
        [coef_b * gram_own + coef_c * quartic_left, coef_b * gram_cross + coef_c * quartic_right], axis=1
    )
    local_rows = jnp.concatenate([own_half, z_other_half], axis=0)
    return coef_a * z_own + bdot(mixer, local_rows, ((1,), (0,)))


def body(embeddings, codes, codebook):
    moved_codes = lax.all_to_all(codes, "sub", split_axis=0, concat_axis=1, tiled=True)
    table = lax.all_gather(codebook, "sub", axis=1, tiled=True)
    decoded = decode_rows(codes, table)
    partial_t = lax.dot_general(
        decoded, embeddings, (((0,), (0,)), ((), ())), preferred_element_type=jnp.float32
    )
    partial_panel = lax.psum_scatter(partial_t, "sub", scatter_dimension=1, tiled=True).T
    code_one_hot = one_hot_codes(moved_codes, table.shape[0])
    counts = jnp.sum(code_one_hot, axis=1, dtype=jnp.float32).T
    core = lax.axis_index("sub") % 2
    panel_rows = partial_panel.shape[0]
    columns = embeddings.reshape(embeddings.shape[0], -1, 2, panel_rows)
    own_columns = lax.dynamic_index_in_dim(columns, core, axis=2, keepdims=False).reshape(embeddings.shape[0], -1)
    other_columns = lax.dynamic_index_in_dim(columns, 1 - core, axis=2, keepdims=False).reshape(embeddings.shape[0], -1)
    partial_panel, moved_codes, counts, own_columns, other_columns = lax.optimization_barrier(
        (partial_panel, moved_codes, counts, own_columns, other_columns)
    )
    cross_panel = rows_sum(partial_panel)
    cross = lax.all_gather(cross_panel, "sub", axis=0, tiled=True)
    width = cross.shape[1]
    frob_scale = jnp.sqrt(jnp.sum(cross * cross)) + frob_eps
    core = lax.axis_index("sub") % 2
    panel_rows = cross.shape[0] // lax.axis_size("sub")
    by_parity = cross.reshape(-1, 2, panel_rows, width)
    z_own = lax.dynamic_index_in_dim(by_parity, core, axis=1, keepdims=False).reshape(-1, width) / frob_scale
    z_other = lax.dynamic_index_in_dim(by_parity, 1 - core, axis=1, keepdims=False).reshape(-1, width) / frob_scale
    z_other_half = z_other.astype(jnp.bfloat16)
    for newton_step_index in range(NS_STEPS - 1):
        z_own = newton_half(z_own, z_other_half)
        z_other_half = partner(z_own.astype(jnp.bfloat16))
    z_own = newton_half(z_own, z_other_half)
    own_half = z_own.astype(jnp.bfloat16)
    z_other_half = partner(own_half)
    rotated = (
        jnp.dot(own_columns, own_half, preferred_element_type=jnp.float32)
        + jnp.dot(other_columns, z_other_half, preferred_element_type=jnp.float32)
    ).astype(jnp.bfloat16)
    moved_rows = lax.all_to_all(rotated, "sub", split_axis=1, concat_axis=0, tiled=True)
    code_sums = codeword_sums(moved_codes, moved_rows, table.shape[0])
    sums_width = code_sums.shape[1]
    totals = rows_sum(jnp.concatenate([code_sums, counts], axis=1))
    code_sums, counts = totals[:, :sums_width], totals[:, sums_width:]
    own_codebook = codebook.astype(jnp.float32)
    spread = jnp.repeat(counts, own_codebook.shape[1] // counts.shape[1], axis=1)
    new_codebook = (code_sums + own_codebook) / (spread + 1.0)
    me = lax.axis_index("sub")
    panel = lax.dynamic_index_in_dim(z_own.reshape(-1, panel_rows, width), me // 2, axis=0, keepdims=False)
    return (panel, rotated, new_codebook)


def solution(mesh):
    in_specs = (P(("rows", "sub"), None), P(None, ("rows", "sub")), P(None, "sub"))
    out_specs = (P("sub", None), P(("rows", "sub"), None), P(None, "sub"))
    return jax.shard_map(body, mesh=mesh, in_specs=in_specs, out_specs=out_specs, check_vma=False)
```

```python
import jax
import jax.numpy as jnp
from jax import lax
from jax.sharding import PartitionSpec as P

NS_STEPS = 3


coef_a = 3.4445
coef_b = -4.775
coef_c = 2.0315
frob_eps = 1e-07


def one_hot_codes(code_block, count_codes):
    levels = lax.broadcasted_iota(jnp.int32, code_block.shape + (count_codes,), 2)
    return (code_block[:, :, None] == levels).astype(jnp.bfloat16)


def decode_rows(codes, table):
    subspaces, local_rows = codes.shape
    count_codes, row_width = table.shape
    sub_width = row_width // subspaces
    codewords = table.reshape(count_codes, subspaces, sub_width)
    one_hot = one_hot_codes(codes, count_codes)
    picked = jnp.einsum("mnk,kmj->nmj", one_hot, codewords, preferred_element_type=jnp.float32)
    return picked.reshape(local_rows, row_width).astype(jnp.bfloat16)


def codeword_sums(codes, row_values, count_codes):
    subspaces, local_rows = codes.shape
    row_width = row_values.shape[1]
    sub_width = row_width // subspaces
    one_hot = one_hot_codes(codes, count_codes)
    pieces = row_values.reshape(local_rows, subspaces, sub_width)
    code_sums = jnp.einsum("mnk,nmj->kmj", one_hot, pieces, preferred_element_type=jnp.float32)
    return code_sums.reshape(count_codes, row_width)


def rows_sum(x):
    groups = lax.axis_size("rows")
    chunk = x.shape[0] // groups
    scattered = lax.all_to_all(x, "rows", split_axis=0, concat_axis=0, tiled=True)
    own = jnp.sum(scattered.reshape((groups, chunk) + x.shape[1:]), axis=0)
    spread = jnp.broadcast_to(own[None], (groups,) + own.shape).reshape(x.shape)
    return lax.all_to_all(spread, "rows", split_axis=0, concat_axis=0, tiled=True)


def panel_rows_sum(x):
    groups = lax.axis_size("rows")
    height, width = x.shape
    tiles = x.reshape(height // 8, 8, 2, width // 2).transpose(0, 2, 1, 3).reshape(groups, 8, width // 2)
    scattered = lax.all_to_all(tiles, "rows", split_axis=0, concat_axis=0, tiled=True)
    own = jnp.sum(scattered, axis=0)
    spread = jnp.broadcast_to(own[None], scattered.shape)
    gathered = lax.all_to_all(spread, "rows", split_axis=0, concat_axis=0, tiled=True)
    return gathered.reshape(height // 8, 2, 8, width // 2).transpose(0, 2, 1, 3).reshape(height, width)


def bdot(left, right, dims):
    return lax.dot_general(
        left.astype(jnp.bfloat16), right.astype(jnp.bfloat16), (dims, ((), ())),
        preferred_element_type=jnp.float32,
    )


def partner(x):
    count = lax.axis_size("sub")
    return lax.ppermute(x, "sub", [(i, i ^ 1) for i in range(count)])


def newton_half(z_own, z_other_half):
    own_half = z_own.astype(jnp.bfloat16)
    gram_own = bdot(own_half, own_half, ((1,), (1,)))
    gram_cross = bdot(own_half, z_other_half, ((1,), (1,)))
    gram_other = partner(gram_own.astype(jnp.bfloat16))
    own_block, cross_block = gram_own.astype(jnp.bfloat16), gram_cross.astype(jnp.bfloat16)
    gram_rows = jnp.concatenate([own_block, cross_block], axis=1)
    quartic_left = bdot(gram_rows, gram_rows, ((1,), (1,)))
    quartic_right = bdot(own_block, cross_block, ((1,), (0,))) + bdot(cross_block, gram_other, ((1,), (0,)))
    mixer = jnp.concatenate(
        [coef_b * gram_own + coef_c * quartic_left, coef_b * gram_cross + coef_c * quartic_right], axis=1
    )
    local_rows = jnp.concatenate([own_half, z_other_half], axis=0)
    return coef_a * z_own + bdot(mixer, local_rows, ((1,), (0,)))


def body(embeddings, codes, codebook):
    moved_codes = lax.all_to_all(codes, "sub", split_axis=0, concat_axis=1, tiled=True)
    table = lax.all_gather(codebook, "sub", axis=1, tiled=True)
    decoded = decode_rows(codes, table)
    partial_t = lax.dot_general(
        decoded, embeddings, (((0,), (0,)), ((), ())), preferred_element_type=jnp.float32
    )
    partial_panel = lax.psum_scatter(partial_t, "sub", scatter_dimension=1, tiled=True).T
    code_one_hot = one_hot_codes(moved_codes, table.shape[0])
    counts = jnp.sum(code_one_hot, axis=1, dtype=jnp.float32).T
    core = lax.axis_index("sub") % 2
    panel_rows = partial_panel.shape[0]
    columns = embeddings.reshape(embeddings.shape[0], -1, 2, panel_rows)
    own_columns = lax.dynamic_index_in_dim(columns, core, axis=2, keepdims=False).reshape(embeddings.shape[0], -1)
    other_columns = lax.dynamic_index_in_dim(columns, 1 - core, axis=2, keepdims=False).reshape(embeddings.shape[0], -1)
    partial_panel, moved_codes, counts, own_columns, other_columns = lax.optimization_barrier(
        (partial_panel, moved_codes, counts, own_columns, other_columns)
    )
    cross_panel = panel_rows_sum(partial_panel)
    cross = lax.all_gather(cross_panel, "sub", axis=0, tiled=True)
    width = cross.shape[1]
    frob_scale = jnp.sqrt(jnp.sum(cross * cross)) + frob_eps
    core = lax.axis_index("sub") % 2
    panel_rows = cross.shape[0] // lax.axis_size("sub")
    by_parity = cross.reshape(-1, 2, panel_rows, width)
    z_own = lax.dynamic_index_in_dim(by_parity, core, axis=1, keepdims=False).reshape(-1, width) / frob_scale
    z_other = lax.dynamic_index_in_dim(by_parity, 1 - core, axis=1, keepdims=False).reshape(-1, width) / frob_scale
    z_other_half = z_other.astype(jnp.bfloat16)
    for newton_step_index in range(NS_STEPS - 1):
        z_own = newton_half(z_own, z_other_half)
        z_other_half = partner(z_own.astype(jnp.bfloat16))
    z_own = newton_half(z_own, z_other_half)
    own_half = z_own.astype(jnp.bfloat16)
    z_other_half = partner(own_half)
    rotated = (
        jnp.dot(own_columns, own_half, preferred_element_type=jnp.float32)
        + jnp.dot(other_columns, z_other_half, preferred_element_type=jnp.float32)
    ).astype(jnp.bfloat16)
    moved_rows = lax.all_to_all(rotated, "sub", split_axis=1, concat_axis=0, tiled=True)
    code_sums = codeword_sums(moved_codes, moved_rows, table.shape[0])
    sums_width = code_sums.shape[1]
    totals = rows_sum(jnp.concatenate([code_sums, counts], axis=1))
    code_sums, counts = totals[:, :sums_width], totals[:, sums_width:]
    own_codebook = codebook.astype(jnp.float32)
    spread = jnp.repeat(counts, own_codebook.shape[1] // counts.shape[1], axis=1)
    new_codebook = (code_sums + own_codebook) / (spread + 1.0)
    me = lax.axis_index("sub")
    panel = lax.dynamic_index_in_dim(z_own.reshape(-1, panel_rows, width), me // 2, axis=0, keepdims=False)
    return (panel, rotated, new_codebook)


def solution(mesh):
    in_specs = (P(("rows", "sub"), None), P(None, ("rows", "sub")), P(None, "sub"))
    out_specs = (P("sub", None), P(("rows", "sub"), None), P(None, "sub"))
    return jax.shard_map(body, mesh=mesh, in_specs=in_specs, out_specs=out_specs, check_vma=False)
```

```python
import jax
import jax.numpy as jnp
from jax import lax
from jax.sharding import PartitionSpec as P

NS_STEPS = 3


coef_a = 3.4445
coef_b = -4.775
coef_c = 2.0315
frob_eps = 1e-07


def one_hot_codes(code_block, count_codes):
    levels = lax.broadcasted_iota(jnp.int32, code_block.shape + (count_codes,), 2)
    return (code_block[:, :, None] == levels).astype(jnp.bfloat16)


def decode_rows(codes, table):
    subspaces, local_rows = codes.shape
    count_codes, row_width = table.shape
    sub_width = row_width // subspaces
    codewords = table.reshape(count_codes, subspaces, sub_width)
    one_hot = one_hot_codes(codes, count_codes)
    picked = jnp.einsum("mnk,kmj->nmj", one_hot, codewords, preferred_element_type=jnp.float32)
    return picked.reshape(local_rows, row_width).astype(jnp.bfloat16)


def codeword_sums(codes, row_values, count_codes):
    subspaces, local_rows = codes.shape
    row_width = row_values.shape[1]
    sub_width = row_width // subspaces
    one_hot = one_hot_codes(codes, count_codes)
    pieces = row_values.reshape(local_rows, subspaces, sub_width)
    code_sums = jnp.einsum("mnk,nmj->kmj", one_hot, pieces, preferred_element_type=jnp.float32)
    return code_sums.reshape(count_codes, row_width)


def rows_sum(x):
    groups = lax.axis_size("rows")
    chunk = x.shape[0] // groups
    scattered = lax.all_to_all(x, "rows", split_axis=0, concat_axis=0, tiled=True)
    own = jnp.sum(scattered.reshape((groups, chunk) + x.shape[1:]), axis=0)
    spread = jnp.broadcast_to(own[None], (groups,) + own.shape).reshape(x.shape)
    return lax.all_to_all(spread, "rows", split_axis=0, concat_axis=0, tiled=True)


def panel_rows_sum(x):
    groups = lax.axis_size("rows")
    height, width = x.shape
    tiles = x.reshape(height // 8, 8, 2, width // 2).transpose(0, 2, 1, 3).reshape(groups, 8, width // 2)
    scattered = lax.all_to_all(tiles, "rows", split_axis=0, concat_axis=0, tiled=True)
    own = jnp.sum(scattered, axis=0)
    spread = jnp.broadcast_to(own[None], scattered.shape)
    gathered = lax.all_to_all(spread, "rows", split_axis=0, concat_axis=0, tiled=True)
    return gathered.reshape(height // 8, 2, 8, width // 2).transpose(0, 2, 1, 3).reshape(height, width)


def bdot(left, right, dims):
    return lax.dot_general(
        left.astype(jnp.bfloat16), right.astype(jnp.bfloat16), (dims, ((), ())),
        preferred_element_type=jnp.float32,
    )


def partner(x):
    count = lax.axis_size("sub")
    return lax.ppermute(x, "sub", [(i, i ^ 1) for i in range(count)])


def newton_half(z_own, z_other_half):
    own_half = z_own.astype(jnp.bfloat16)
    gram_own = bdot(own_half, own_half, ((1,), (1,)))
    gram_cross = bdot(own_half, z_other_half, ((1,), (1,)))
    gram_other = partner(gram_own.astype(jnp.bfloat16))
    own_block, cross_block = gram_own.astype(jnp.bfloat16), gram_cross.astype(jnp.bfloat16)
    gram_rows = jnp.concatenate([own_block, cross_block], axis=1)
    quartic_left = bdot(gram_rows, gram_rows, ((1,), (1,)))
    quartic_right = bdot(own_block, cross_block, ((1,), (0,))) + bdot(cross_block, gram_other, ((1,), (0,)))
    mixer = jnp.concatenate(
        [coef_b * gram_own + coef_c * quartic_left, coef_b * gram_cross + coef_c * quartic_right], axis=1
    )
    local_rows = jnp.concatenate([own_half, z_other_half], axis=0)
    return coef_a * z_own + bdot(mixer, local_rows, ((1,), (0,)))


def body(embeddings, codes, codebook):
    moved_codes = lax.all_to_all(codes, "sub", split_axis=0, concat_axis=1, tiled=True)
    table = lax.all_gather(codebook, "sub", axis=1, tiled=True)
    decoded = decode_rows(codes, table)
    partial_t = lax.dot_general(
        decoded, embeddings, (((0,), (0,)), ((), ())), preferred_element_type=jnp.float32
    )
    partial_panel = lax.psum_scatter(partial_t, "sub", scatter_dimension=1, tiled=True).T
    code_one_hot = one_hot_codes(moved_codes, table.shape[0])
    counts = jnp.sum(code_one_hot, axis=1, dtype=jnp.float32).T
    core = lax.axis_index("sub") % 2
    panel_rows = partial_panel.shape[0]
    columns = embeddings.reshape(embeddings.shape[0], -1, 2, panel_rows)
    own_columns = lax.dynamic_index_in_dim(columns, core, axis=2, keepdims=False).reshape(embeddings.shape[0], -1)
    other_columns = lax.dynamic_index_in_dim(columns, 1 - core, axis=2, keepdims=False).reshape(embeddings.shape[0], -1)
    partial_panel, moved_codes, counts, own_columns, other_columns = lax.optimization_barrier(
        (partial_panel, moved_codes, counts, own_columns, other_columns)
    )
    cross_panel = panel_rows_sum(partial_panel)
    cross = lax.all_gather(cross_panel, "sub", axis=0, tiled=True)
    width = cross.shape[1]
    frob_scale = jnp.sqrt(jnp.sum(cross * cross)) + frob_eps
    core = lax.axis_index("sub") % 2
    panel_rows = cross.shape[0] // lax.axis_size("sub")
    by_parity = cross.reshape(-1, 2, panel_rows, width)
    z_own = lax.dynamic_index_in_dim(by_parity, core, axis=1, keepdims=False).reshape(-1, width) / frob_scale
    z_other = lax.dynamic_index_in_dim(by_parity, 1 - core, axis=1, keepdims=False).reshape(-1, width) / frob_scale
    z_other_half = z_other.astype(jnp.bfloat16)
    for newton_step_index in range(NS_STEPS - 1):
        z_own = newton_half(z_own, z_other_half)
        z_other_half = partner(z_own.astype(jnp.bfloat16))
    z_own = newton_half(z_own, z_other_half)
    own_half = z_own.astype(jnp.bfloat16)
    z_other_half = partner(own_half)
    rotated = (
        jnp.dot(own_columns, own_half, preferred_element_type=jnp.float32)
        + jnp.dot(other_columns, z_other_half, preferred_element_type=jnp.float32)
    ).astype(jnp.bfloat16)
    moved_rows = lax.all_to_all(rotated, "sub", split_axis=1, concat_axis=0, tiled=True)
    code_sums = codeword_sums(moved_codes, moved_rows, table.shape[0])
    sums_width = code_sums.shape[1]
    padded_counts = jnp.pad(counts, ((0, 0), (0, sums_width - counts.shape[1])))
    totals = rows_sum(jnp.concatenate([code_sums, padded_counts], axis=1))
    code_sums, counts = totals[:, :sums_width], totals[:, sums_width:sums_width + counts.shape[1]]
    own_codebook = codebook.astype(jnp.float32)
    spread = jnp.repeat(counts, own_codebook.shape[1] // counts.shape[1], axis=1)
    new_codebook = (code_sums + own_codebook) / (spread + 1.0)
    me = lax.axis_index("sub")
    panel = lax.dynamic_index_in_dim(z_own.reshape(-1, panel_rows, width), me // 2, axis=0, keepdims=False)
    return (panel, rotated, new_codebook)


def solution(mesh):
    in_specs = (P(("rows", "sub"), None), P(None, ("rows", "sub")), P(None, "sub"))
    out_specs = (P("sub", None), P(("rows", "sub"), None), P(None, "sub"))
    return jax.shard_map(body, mesh=mesh, in_specs=in_specs, out_specs=out_specs, check_vma=False)
```
